256 devices in a mesh: group: 8 (over z), dom: 32 (over x, y, core).
Axes of the slice: x: 4, y: 4, z: 8, core: 2. Of those that a mesh axis runs over, the one named last changes fastest.
Arguments:
- feats: bfloat16 [32768, 1024], P(('group', 'dom')), may hold values from -6 to 6
- history: bfloat16 [32768, 1024], P(('group', 'dom')), may hold values from -0.25 to 2
- grad_out: bfloat16 [32768, 1024], P(('group', 'dom')), may hold values from -24 to 24
- w_first: bfloat16 [1024, 1024], replicated, may hold values from -0.1875 to 0.1875
- w_second: bfloat16 [1024, 1024], replicated, may hold values from -0.1875 to 0.1875
- send_index: int32 [256, 32, 16], P(('group', 'dom')), may hold values from 0 to 127, as said below
- halo_index: int32 [131072], P(('group', 'dom')), may hold values from 0 to 511
- hub_rows: int32 [256, 32], P(('group', 'dom')), may hold values from 0 to 127
- tile_cols: int32 [256, 4], P(('group', 'dom')), may hold values from 0 to 6
- tile_vals: bfloat16 [256, 4, 128, 128], P(('group', 'dom')), may hold values from -0.25 to 0.25
Outputs:
- new_history: bfloat16 [32768, 1024], P(('group', 'dom'))
- embed_grad: bfloat16 [32768, 1024], P(('group', 'dom'))
- grad_first: float32 [1024, 1024], P(('group', 'dom'))
- grad_second: float32 [1024, 1024], P(('group', 'dom'))
The draws below stay inside these ranges and needn't reach their ends.
Inputs may be any that keep to these rules, and one draw needn't show every extreme that they name: `send_index`: for each device and each dom peer the 16 rows are distinct. `halo_index`: A value q names slot q % 16 of the rows received from dom peer q // 16 of the same group; values may repeat. `hub_rows`: rows may repeat. `tile_cols`: source tile 0 is the device's own rows, tiles 1 to 4 are halo tiles, tiles 5 and 6 are hub tiles; values may repeat in a row.
All inputs are finite; a program needn't handle non-finite values.
Results may differ from the reference program's by a relative error of at most 0.006.
Values may be sent and summed in bfloat16 or wider, within the bound.
No kernel may reach another device: no remote copies, remote signals or barrier semaphores. Data moves between devices by JAX's collectives and lax.ppermute only.
A program may use at most 64 MiB of HBM per device.

```python
import math
import jax
import jax.numpy as jnp
import numpy as np
from jax import lax

D = 1024
V_DEV = 128
TILE = 128
TPR = 4
CAP = 16
HALO = 512
HUB_DEV = 32
VERTS = 32768
RT_DEV = 1
RTILES = 256
SLOTS = 512
SRC = 896
ST = 7
N_GROUP = 8
N_DOM = 32
DEVICES = 256


def draw_send_index(key, part):
    scores = jax.random.randint(key, (DEVICES, N_DOM, V_DEV), 0, 2 ** 16)
    scores = scores * V_DEV + jnp.arange(V_DEV, dtype=jnp.int32)[None, None, :]
    ranking = jnp.argsort(scores, axis=-1, stable=True)
    return ranking[:, :, :CAP].astype(jnp.int32)


def place_ends(array, stream_key, low, top_value):
    extent = array.shape
    index_at = [jax.random.randint(jax.random.fold_in(stream_key, axis), (), 0, extent[axis]) for axis in range(len(extent))]
    array = array.at[tuple(index_at)].set(low)
    longest = extent.index(max(extent))
    index_at[longest] = (index_at[longest] + 1) % extent[longest]
    return array.at[tuple(index_at)].set(top_value)


def spiked(drawn, key, source, target, blocks, factor):
    owner, partner = [(jnp.arange(drawn.shape[dim]) // (drawn.shape[dim] // blocks)).reshape([-1 if axis == dim else 1 for axis in range(drawn.ndim)]) for dim in (source, target)]
    chosen = jax.random.permutation(key, blocks)[partner]
    strong = (owner == chosen) | (owner == (partner + blocks // 2) % blocks)
    return jnp.where(strong, factor * drawn, drawn)


def level_of(own_key, dims, split, smallest, top_value):
    def one(dim, parts):
        steps = jax.random.uniform(jax.random.fold_in(jax.random.fold_in(own_key, 6), dim), (parts,), jnp.float32, smallest / len(split), top_value / len(split))
        return jnp.repeat(jnp.exp(steps), dims[dim] // parts).reshape((-1,) + (1,) * (len(dims) - dim - 1))

    loudness = one(*split[0])
    for cut in split[1:]:
        loudness = loudness * one(*cut)
    return loudness


def rank_bounds(amount, slope):
    weights = [(1 << 20) // math.isqrt(grade ** slope) + 1 for grade in range(1, amount + 1)]
    width = 1 + sum(weights) // (1 << 30)
    return np.cumsum(np.array([max(1, weight // width) for weight in weights]))


def ranked_ids(stream_key, shape, amount, lean):
    table = rank_bounds(amount, lean)
    pick = jax.random.randint(jax.random.fold_in(stream_key, 1), shape, 0, int(table[amount - 1]))
    rank = jnp.searchsorted(jnp.asarray(table, jnp.int32), pick, side="right")
    return jax.random.permutation(jax.random.fold_in(stream_key, 2), amount)[rank].astype(jnp.int32)


def centred(own_key, shape, deviation, bound, cuts=(), kind=jnp.bfloat16):
    drawn = jax.random.normal(own_key, shape, jnp.float32) * deviation
    if len(cuts) > 0:
        drawn = level_of(own_key, shape, cuts, -0.22, 0.18) * drawn
    return jnp.clip(drawn, min=-bound, max=bound).astype(kind)


def bell_draw_with(own_key, extent, scale, most, split, heavy, held_as=jnp.bfloat16):
    result = scale * jax.random.normal(own_key, extent, jnp.float32)
    if split:
        result = result * level_of(own_key, extent, split, -0.22, 0.18)
    return jnp.clip(spiked(result, jax.random.fold_in(own_key, 3), *heavy), -most, most).astype(held_as)


def setup_inputs(seed: int = 0) -> dict:
    key_of = jax.random.split(jax.random.key(seed), 11)
    return {
        "feats": centred(key_of[0], (VERTS, D), 1.0, 6.0, ((0, 256),)),
        "history": jnp.clip(-0.25 + 2.25 * jax.random.uniform(key_of[1], (VERTS, D), jnp.float32) ** level_of(key_of[1], (VERTS, D), ((0, 256),), -0.2, 0.2), -0.25, 2.0).astype(jnp.bfloat16),
        "grad_out": bell_draw_with(key_of[2], (VERTS, D), 1.0, 24.0, ((0, 256),), (0, 1, 256, 6.0)),
        "w_first": centred(key_of[3], (D, D), D ** -0.5, 0.1875),
        "w_second": centred(key_of[4], (D, D), D ** -0.5, 0.1875),
        "send_index": draw_send_index(jax.random.fold_in(key_of[10], 71), 0),
        "halo_index": place_ends(ranked_ids(key_of[6], (DEVICES * HALO,), SLOTS, 2), jax.random.fold_in(key_of[6], 3), 0, SLOTS - 1).astype(jnp.int32),
        "hub_rows": place_ends(jax.random.randint(key_of[7], (DEVICES, HUB_DEV), 0, V_DEV), jax.random.fold_in(key_of[7], 1), 0, V_DEV - 1).astype(jnp.int32),
        "tile_cols": place_ends(jax.random.randint(key_of[8], (RTILES, TPR), 0, ST), jax.random.fold_in(key_of[8], 1), 0, ST - 1).astype(jnp.int32),
        "tile_vals": centred(key_of[9], (RTILES, TPR, TILE, TILE), (TPR * TILE) ** -0.5, 0.25, ((0, 256),)),
    }


def source_table(send_index, halo_index, hub_rows):
    blocks = jnp.arange(DEVICES, dtype=jnp.int32)
    dom_of = blocks % N_DOM
    own_rows = blocks[:, None] * V_DEV + jnp.arange(V_DEV, dtype=jnp.int32)[None, :]
    row_base = (jnp.arange(N_GROUP, dtype=jnp.int32)[:, None] * N_DOM + jnp.arange(N_DOM, dtype=jnp.int32)[None, :]) * V_DEV
    sent_rows = send_index.reshape(N_GROUP, N_DOM, N_DOM, CAP) + row_base[:, :, None, None]
    received = jnp.transpose(sent_rows, (0, 2, 1, 3)).reshape(DEVICES, N_DOM * CAP)
    halo_ids = jnp.take_along_axis(received, halo_index.reshape(DEVICES, HALO), axis=1)
    hub_ids = hub_rows.reshape(N_GROUP, N_DOM, HUB_DEV) + row_base[:, :, None]
    hub_panel = jnp.transpose(hub_ids, (1, 0, 2)).reshape(N_DOM, N_GROUP * HUB_DEV)
    hub_all = hub_panel[dom_of]
    return jnp.concatenate([own_rows, halo_ids, hub_all], axis=1).astype(jnp.int32)

def aggregate(table, halo_table, source_ids, tile_cols, tile_vals):
    tile_ids = tile_cols.reshape(DEVICES, RT_DEV, TPR)
    tile_weights = tile_vals.reshape(DEVICES, RT_DEV, TPR, TILE, TILE)
    position = jnp.arange(SRC, dtype=jnp.int32)
    in_halo = (position >= V_DEV) & (position < V_DEV + HALO)

    def per_block(inputs):
        block_ids, block_tiles, block_weights = inputs
        source = jnp.where(in_halo[:, None], halo_table[block_ids], table[block_ids]).reshape(ST, TILE, D)
        picked = source[block_tiles].astype(jnp.float32)
        summed = jnp.einsum('rtij,rtjd->rid', block_weights.astype(jnp.float32), picked, precision=lax.Precision.HIGHEST)
        return summed.reshape(V_DEV, D).astype(jnp.bfloat16)
    return lax.map(per_block, (source_ids, tile_ids, tile_weights)).reshape(VERTS, D)

def spread_back(agg_grad, source_ids, tile_cols, tile_vals):
    tile_ids = tile_cols.reshape(DEVICES, RT_DEV, TPR)
    tile_weights = tile_vals.reshape(DEVICES, RT_DEV, TPR, TILE, TILE)
    kept_rows = jnp.concatenate([jnp.arange(V_DEV, dtype=jnp.int32), jnp.arange(V_DEV + HALO, SRC, dtype=jnp.int32)])

    def per_block(inputs):
        block_tiles, block_weights, grad_rows = inputs
        tile_terms = jnp.einsum('rtij,rid->rtjd', block_weights.astype(jnp.float32), grad_rows.reshape(RT_DEV, TILE, D).astype(jnp.float32), precision=lax.Precision.HIGHEST)
        spread = jnp.zeros((ST, TILE, D), jnp.float32).at[block_tiles].add(tile_terms)
        return spread.reshape(SRC, D)[kept_rows]
    block_grads = lax.map(per_block, (tile_ids, tile_weights, agg_grad.reshape(DEVICES, V_DEV, D)))
    target_ids = source_ids[:, kept_rows]
    return jnp.zeros((VERTS, D), jnp.float32).at[target_ids.reshape(-1)].add(block_grads.reshape(-1, D))

def reference(feats, history, grad_out, w_first, w_second, send_index, halo_index, hub_rows, tile_cols, tile_vals):
    source_ids = source_table(send_index, halo_index, hub_rows)
    agg_first = aggregate(feats, feats, source_ids, tile_cols, tile_vals)
    z_first = jnp.dot(agg_first, w_first, preferred_element_type=jnp.float32)
    new_history = jax.nn.silu(z_first).astype(jnp.bfloat16)
    agg_second = aggregate(new_history, history, source_ids, tile_cols, tile_vals)
    factor = 1.0 / math.sqrt(VERTS)
    grad_second = jnp.dot(grad_out.T, agg_second, preferred_element_type=jnp.float32) * factor
    agg_grad = jnp.dot(grad_out, w_second.T, preferred_element_type=jnp.float32).astype(jnp.bfloat16)
    vertex_grad = spread_back(agg_grad, source_ids, tile_cols, tile_vals)
    gate_value = jax.nn.sigmoid(z_first)
    dz_first = (vertex_grad * gate_value * (1.0 + z_first * (1.0 - gate_value))).astype(jnp.bfloat16)
    grad_first = jnp.dot(dz_first.T, agg_first, preferred_element_type=jnp.float32) * factor
    return (new_history, vertex_grad.astype(jnp.bfloat16), grad_first, grad_second)
```

```python
import math

import jax
import jax.numpy as jnp
from jax import lax
from jax.sharding import PartitionSpec as P

D = 1024
V_DEV = 128
TILE = 128
HALO = 512


def combine_tiles(own_rows, halo_rows, hub_panel, tile_cols, tile_vals):
    source = jnp.concatenate([own_rows, halo_rows, hub_panel], axis=0)
    feature_width = source.shape[1]
    picked = source.reshape(-1, tile_vals.shape[2], feature_width)[tile_cols]
    summed = jnp.einsum("rtij,rtjd->rid", tile_vals, picked, preferred_element_type=jnp.float32)
    return summed.reshape(-1, feature_width).astype(jnp.bfloat16)


def weight_product(left_rows, right_rows):
    return lax.dot_general(
        left_rows, right_rows, (((0,), (0,)), ((), ())), preferred_element_type=jnp.float32
    )


def reduce_weight(product, rows_per_device):
    factor = 1.0 / math.sqrt(rows_per_device * lax.axis_size("group") * lax.axis_size("dom"))
    n_dom = lax.axis_size("dom")
    in_group = lax.psum_scatter(product, "group", scatter_dimension=0, tiled=True)
    pieces = lax.all_to_all(
        in_group.reshape(n_dom, -1, in_group.shape[1]), "dom", split_axis=0, concat_axis=0, tiled=True
    )
    return pieces.sum(axis=0) * factor


def gather_hubs(hub_rows):
    n_group = lax.axis_size("group")
    copies = jnp.broadcast_to(hub_rows[None], (n_group,) + hub_rows.shape)
    spread = lax.all_to_all(copies, "group", split_axis=0, concat_axis=0, tiled=True)
    return spread.reshape(-1, hub_rows.shape[1])


def on_device(
    feats,
    history,
    grad_out,
    w_first,
    w_second,
    send_index,
    halo_index,
    hub_rows,
    tile_cols,
    tile_vals,
):
    routes = send_index[0]
    owned_hubs = hub_rows[0]
    rows = feats.shape[0]

    agg_grad = lax.dot_general(
        grad_out, w_second, (((1,), (1,)), ((), ())), preferred_element_type=jnp.float32
    ).astype(jnp.bfloat16)
    n_hub = lax.axis_size("group") * owned_hubs.shape[0]
    source_tiles = (V_DEV + HALO + n_hub) // TILE
    tile_terms = jnp.einsum(
        "rtij,rid->rtjd",
        tile_vals,
        agg_grad.reshape(-1, TILE, D),
        preferred_element_type=jnp.float32,
    )
    selector = (
        tile_cols[:, :, None] == jnp.arange(source_tiles, dtype=jnp.int32)[None, None, :]
    ).astype(jnp.float32)
    spread = jnp.einsum(
        "rts,rtjd->sjd", selector, tile_terms, precision=lax.Precision.HIGHEST
    ).reshape(-1, D)
    own_grad = spread[:V_DEV]
    hub_grad = lax.psum_scatter(spread[V_DEV + HALO :], "group", scatter_dimension=0, tiled=True)
    vertex_grad = own_grad.at[owned_hubs].add(hub_grad)

    feat_slots = lax.all_to_all(feats[routes], "dom", split_axis=0, concat_axis=0, tiled=True)
    hist_slots = lax.all_to_all(history[routes], "dom", split_axis=0, concat_axis=0, tiled=True)
    hub_first = gather_hubs(feats[owned_hubs])
    feat_halo = feat_slots.reshape(-1, D)[halo_index]
    agg_first = combine_tiles(feats, feat_halo, hub_first, tile_cols, tile_vals)
    z_first = jnp.dot(agg_first, w_first, preferred_element_type=jnp.float32)
    new_history = jax.nn.silu(z_first).astype(jnp.bfloat16)
    gate_value = jax.nn.sigmoid(z_first)
    dz_first = (vertex_grad * gate_value * (1.0 + z_first * (1.0 - gate_value))).astype(
        jnp.bfloat16
    )
    product_first = weight_product(dz_first, agg_first)
    product_first, new_history = lax.optimization_barrier((product_first, new_history))
    grad_first = reduce_weight(product_first, rows)

    hist_halo = hist_slots.reshape(-1, D)[halo_index]
    hub_second = gather_hubs(new_history[owned_hubs])
    agg_second = combine_tiles(new_history, hist_halo, hub_second, tile_cols, tile_vals)
    grad_second = reduce_weight(weight_product(grad_out, agg_second), rows)
    return (new_history, vertex_grad.astype(jnp.bfloat16), grad_first, grad_second)


def solution(mesh):
    placed = (
        P(("group", "dom"), None),
        P(("group", "dom"), None),
        P(("group", "dom"), None),
        P(),
        P(),
        P(("group", "dom"), None, None),
        P(("group", "dom")),
        P(("group", "dom"), None),
        P(("group", "dom"), None),
        P(("group", "dom"), None, None, None),
    )
    return jax.shard_map(
        on_device,
        mesh=mesh,
        in_specs=placed,
        out_specs=(
            P(("group", "dom"), None),
            P(("group", "dom"), None),
            P(("group", "dom"), None),
            P(("group", "dom"), None),
        ),
        check_vma=False,
    )
```

```python
import math

import jax
import jax.numpy as jnp
from jax import lax
from jax.sharding import PartitionSpec as P

D = 1024
V_DEV = 128
TILE = 128
HALO = 512


def combine_tiles(own_rows, halo_rows, hub_panel, tile_cols, tile_vals):
    source = jnp.concatenate([own_rows, halo_rows, hub_panel], axis=0)
    feature_width = source.shape[1]
    picked = source.reshape(-1, tile_vals.shape[2], feature_width)[tile_cols]
    summed = jnp.einsum("rtij,rtjd->rid", tile_vals, picked, preferred_element_type=jnp.float32)
    return summed.reshape(-1, feature_width).astype(jnp.bfloat16)


def weight_product(left_rows, right_rows):
    return lax.dot_general(
        left_rows, right_rows, (((0,), (0,)), ((), ())), preferred_element_type=jnp.float32
    )


def reduce_weight(product, rows_per_device):
    factor = 1.0 / math.sqrt(rows_per_device * lax.axis_size("group") * lax.axis_size("dom"))
    n_group = lax.axis_size("group")
    n_dom = lax.axis_size("dom")
    width = product.shape[1]
    blocks = product.reshape(n_group, n_dom // 2, 2, -1, width)
    core = lax.axis_index("dom") % 2
    keep = lax.dynamic_index_in_dim(blocks, core, axis=2, keepdims=False)
    give = lax.dynamic_index_in_dim(blocks, 1 - core, axis=2, keepdims=False)
    pair = keep + lax.ppermute(give, "dom", [(i, i ^ 1) for i in range(n_dom)])
    in_group = lax.psum_scatter(pair, "group", scatter_dimension=0, tiled=True)
    chunks = in_group.reshape(n_dom // 2, 1, -1, width)
    slot = jnp.arange(2, dtype=jnp.int32)[None, :, None, None] == core
    outgoing = jnp.where(slot, chunks, 0.0).reshape(n_dom, -1, width)
    pieces = lax.all_to_all(outgoing, "dom", split_axis=0, concat_axis=0, tiled=True)
    return pieces.sum(axis=0) * factor


def gather_hubs(hub_rows):
    n_group = lax.axis_size("group")
    copies = jnp.broadcast_to(hub_rows[None], (n_group,) + hub_rows.shape)
    spread = lax.all_to_all(copies, "group", split_axis=0, concat_axis=0, tiled=True)
    return spread.reshape(-1, hub_rows.shape[1])


def on_device(
    feats,
    history,
    grad_out,
    w_first,
    w_second,
    send_index,
    halo_index,
    hub_rows,
    tile_cols,
    tile_vals,
):
    routes = send_index[0]
    owned_hubs = hub_rows[0]
    rows = feats.shape[0]

    agg_grad = lax.dot_general(
        grad_out, w_second, (((1,), (1,)), ((), ())), preferred_element_type=jnp.float32
    ).astype(jnp.bfloat16)
    n_hub = lax.axis_size("group") * owned_hubs.shape[0]
    source_tiles = (V_DEV + HALO + n_hub) // TILE
    tile_terms = jnp.einsum(
        "rtij,rid->rtjd",
        tile_vals,
        agg_grad.reshape(-1, TILE, D),
        preferred_element_type=jnp.float32,
    )
    selector = (
        tile_cols[:, :, None] == jnp.arange(source_tiles, dtype=jnp.int32)[None, None, :]
    ).astype(jnp.float32)
    spread = jnp.einsum(
        "rts,rtjd->sjd", selector, tile_terms, precision=lax.Precision.HIGHEST
    ).reshape(-1, D)
    own_grad = spread[:V_DEV]
    hub_grad = lax.psum_scatter(spread[V_DEV + HALO :], "group", scatter_dimension=0, tiled=True)
    vertex_grad = own_grad.at[owned_hubs].add(hub_grad)

    both_slots = lax.all_to_all(
        jnp.stack([feats[routes], history[routes]], axis=1), "dom", split_axis=0, concat_axis=0, tiled=True
    )
    feat_slots = both_slots[:, 0]
    hist_slots = both_slots[:, 1]
    hub_first = gather_hubs(feats[owned_hubs])
    feat_halo = feat_slots.reshape(-1, D)[halo_index]
    agg_first = combine_tiles(feats, feat_halo, hub_first, tile_cols, tile_vals)
    z_first = jnp.dot(agg_first, w_first, preferred_element_type=jnp.float32)
    new_history = jax.nn.silu(z_first).astype(jnp.bfloat16)
    gate_value = jax.nn.sigmoid(z_first)
    dz_first = (vertex_grad * gate_value * (1.0 + z_first * (1.0 - gate_value))).astype(
        jnp.bfloat16
    )
    product_first = weight_product(dz_first, agg_first)
    product_first, new_history = lax.optimization_barrier((product_first, new_history))
    grad_first = reduce_weight(product_first, rows)

    hist_halo = hist_slots.reshape(-1, D)[halo_index]
    hub_second = gather_hubs(new_history[owned_hubs])
    agg_second = combine_tiles(new_history, hist_halo, hub_second, tile_cols, tile_vals)
    grad_second = reduce_weight(weight_product(grad_out, agg_second), rows)
    return (new_history, vertex_grad.astype(jnp.bfloat16), grad_first, grad_second)


def solution(mesh):
    placed = (
        P(("group", "dom"), None),
        P(("group", "dom"), None),
        P(("group", "dom"), None),
        P(),
        P(),
        P(("group", "dom"), None, None),
        P(("group", "dom")),
        P(("group", "dom"), None),
        P(("group", "dom"), None),
        P(("group", "dom"), None, None, None),
    )
    return jax.shard_map(
        on_device,
        mesh=mesh,
        in_specs=placed,
        out_specs=(
            P(("group", "dom"), None),
            P(("group", "dom"), None),
            P(("group", "dom"), None),
            P(("group", "dom"), None),
        ),
        check_vma=False,
    )
```

```python
import math

import jax
import jax.numpy as jnp
from jax import lax
from jax.sharding import PartitionSpec as P

D = 1024
V_DEV = 128
TILE = 128
HALO = 512


def combine_tiles(own_rows, halo_rows, hub_panel, tile_cols, tile_vals):
    source = jnp.concatenate([own_rows, halo_rows, hub_panel], axis=0)
    feature_width = source.shape[1]
    picked = source.reshape(-1, tile_vals.shape[2], feature_width)[tile_cols]
    summed = jnp.einsum("rtij,rtjd->rid", tile_vals, picked, preferred_element_type=jnp.float32)
    return summed.reshape(-1, feature_width).astype(jnp.bfloat16)


def weight_product(left_rows, right_rows):
    return lax.dot_general(
        left_rows, right_rows, (((0,), (0,)), ((), ())), preferred_element_type=jnp.float32
    )


def pair_product(left_rows, right_rows):
    n_group = lax.axis_size("group")
    n_dom = lax.axis_size("dom")
    core = lax.axis_index("dom") % 2
    columns = left_rows.reshape(left_rows.shape[0], n_group, n_dom // 2, 2, -1)
    keep = lax.dynamic_index_in_dim(columns, core, axis=3, keepdims=False)
    give = lax.dynamic_index_in_dim(columns, 1 - core, axis=3, keepdims=False)
    kept = weight_product(keep.reshape(left_rows.shape[0], -1), right_rows)
    sent = weight_product(give.reshape(left_rows.shape[0], -1), right_rows)
    return kept + lax.ppermute(sent, "dom", [(i, i ^ 1) for i in range(n_dom)])


def reduce_weight(pair, rows_per_device):
    factor = 1.0 / math.sqrt(rows_per_device * lax.axis_size("group") * lax.axis_size("dom"))
    n_group = lax.axis_size("group")
    n_dom = lax.axis_size("dom")
    width = pair.shape[1]
    core = lax.axis_index("dom") % 2
    in_group = lax.psum_scatter(pair.reshape(n_group, -1, width), "group", scatter_dimension=0, tiled=True)
    chunks = in_group.reshape(n_dom // 2, 1, -1, width)
    slot = jnp.arange(2, dtype=jnp.int32)[None, :, None, None] == core
    outgoing = jnp.where(slot, chunks, 0.0).reshape(n_dom, -1, width)
    pieces = lax.all_to_all(outgoing, "dom", split_axis=0, concat_axis=0, tiled=True)
    return pieces.sum(axis=0) * factor


def gather_hubs(hub_rows):
    n_group = lax.axis_size("group")
    copies = jnp.broadcast_to(hub_rows[None], (n_group,) + hub_rows.shape)
    spread = lax.all_to_all(copies, "group", split_axis=0, concat_axis=0, tiled=True)
    return spread.reshape(-1, hub_rows.shape[1])


def on_device(
    feats,
    history,
    grad_out,
    w_first,
    w_second,
    send_index,
    halo_index,
    hub_rows,
    tile_cols,
    tile_vals,
):
    routes = send_index[0]
    owned_hubs = hub_rows[0]
    rows = feats.shape[0]

    agg_grad = lax.dot_general(
        grad_out, w_second, (((1,), (1,)), ((), ())), preferred_element_type=jnp.float32
    ).astype(jnp.bfloat16)
    n_hub = lax.axis_size("group") * owned_hubs.shape[0]
    source_tiles = (V_DEV + HALO + n_hub) // TILE
    tile_terms = jnp.einsum(
        "rtij,rid->rtjd",
        tile_vals,
        agg_grad.reshape(-1, TILE, D),
        preferred_element_type=jnp.float32,
    )
    selector = (
        tile_cols[:, :, None] == jnp.arange(source_tiles, dtype=jnp.int32)[None, None, :]
    ).astype(jnp.float32)
    spread = jnp.einsum(
        "rts,rtjd->sjd", selector, tile_terms, precision=lax.Precision.HIGHEST
    ).reshape(-1, D)
    own_grad = spread[:V_DEV]
    hub_grad = lax.psum_scatter(spread[V_DEV + HALO :], "group", scatter_dimension=0, tiled=True)
    vertex_grad = own_grad.at[owned_hubs].add(hub_grad)

    both_slots = lax.all_to_all(
        jnp.stack([feats[routes], history[routes]], axis=1), "dom", split_axis=0, concat_axis=0, tiled=True
    )
    feat_slots = both_slots[:, 0]
    hist_slots = both_slots[:, 1]
    hub_first = gather_hubs(feats[owned_hubs])
    feat_halo = feat_slots.reshape(-1, D)[halo_index]
    agg_first = combine_tiles(feats, feat_halo, hub_first, tile_cols, tile_vals)
    z_first = jnp.dot(agg_first, w_first, preferred_element_type=jnp.float32)
    new_history = jax.nn.silu(z_first).astype(jnp.bfloat16)
    gate_value = jax.nn.sigmoid(z_first)
    dz_first = (vertex_grad * gate_value * (1.0 + z_first * (1.0 - gate_value))).astype(
        jnp.bfloat16
    )
    product_first = pair_product(dz_first, agg_first)
    product_first, new_history = lax.optimization_barrier((product_first, new_history))
    grad_first = reduce_weight(product_first, rows)

    hist_halo = hist_slots.reshape(-1, D)[halo_index]
    hub_second = gather_hubs(new_history[owned_hubs])
    agg_second = combine_tiles(new_history, hist_halo, hub_second, tile_cols, tile_vals)
    grad_second = reduce_weight(pair_product(grad_out, agg_second), rows)
    return (new_history, vertex_grad.astype(jnp.bfloat16), grad_first, grad_second)


def solution(mesh):
    placed = (
        P(("group", "dom"), None),
        P(("group", "dom"), None),
        P(("group", "dom"), None),
        P(),
        P(),
        P(("group", "dom"), None, None),
        P(("group", "dom")),
        P(("group", "dom"), None),
        P(("group", "dom"), None),
        P(("group", "dom"), None, None, None),
    )
    return jax.shard_map(
        on_device,
        mesh=mesh,
        in_specs=placed,
        out_specs=(
            P(("group", "dom"), None),
            P(("group", "dom"), None),
            P(("group", "dom"), None),
            P(("group", "dom"), None),
        ),
        check_vma=False,
    )
```

```python
import math

import jax
import jax.numpy as jnp
from jax import lax
from jax.sharding import PartitionSpec as P

D = 1024
V_DEV = 128
TILE = 128
HALO = 512


def combine_tiles(own_rows, halo_rows, hub_panel, tile_cols, tile_vals):
    source = jnp.concatenate([own_rows, halo_rows, hub_panel], axis=0)
    feature_width = source.shape[1]
    picked = source.reshape(-1, tile_vals.shape[2], feature_width)[tile_cols]
    summed = jnp.einsum("rtij,rtjd->rid", tile_vals, picked, preferred_element_type=jnp.float32)
    return summed.reshape(-1, feature_width).astype(jnp.bfloat16)


def weight_product(left_rows, right_rows):
    return lax.dot_general(
        left_rows, right_rows, (((0,), (0,)), ((), ())), preferred_element_type=jnp.float32
    )


def pair_product(left_rows, right_rows):
    n_group = lax.axis_size("group")
    n_dom = lax.axis_size("dom")
    core = lax.axis_index("dom") % 2
    columns = left_rows.reshape(left_rows.shape[0], n_group, n_dom // 2, 2, -1)
    keep = lax.dynamic_index_in_dim(columns, core, axis=3, keepdims=False)
    give = lax.dynamic_index_in_dim(columns, 1 - core, axis=3, keepdims=False)
    kept = weight_product(keep.reshape(left_rows.shape[0], -1), right_rows)
    sent = weight_product(give.reshape(left_rows.shape[0], -1), right_rows)
    return kept + lax.ppermute(sent, "dom", [(i, i ^ 1) for i in range(n_dom)])


def reduce_in_group(pair):
    n_group = lax.axis_size("group")
    n_dom = lax.axis_size("dom")
    width = pair.shape[1]
    core = lax.axis_index("dom") % 2
    in_group = lax.psum_scatter(pair.reshape(n_group, -1, width), "group", scatter_dimension=0, tiled=True)
    chunks = in_group.reshape(n_dom // 2, 1, -1, width)
    slot = jnp.arange(2, dtype=jnp.int32)[None, :, None, None] == core
    return jnp.where(slot, chunks, 0.0).reshape(n_dom, -1, width)


def reduce_over_dom(outgoing, rows_per_device):
    factor = 1.0 / math.sqrt(rows_per_device * lax.axis_size("group") * lax.axis_size("dom"))
    pieces = lax.all_to_all(outgoing, "dom", split_axis=0, concat_axis=0, tiled=True)
    return pieces.sum(axis=0) * factor


def gather_hubs(hub_rows):
    n_group = lax.axis_size("group")
    copies = jnp.broadcast_to(hub_rows[None], (n_group,) + hub_rows.shape)
    spread = lax.all_to_all(copies, "group", split_axis=0, concat_axis=0, tiled=True)
    return spread.reshape(-1, hub_rows.shape[1])


def on_device(
    feats,
    history,
    grad_out,
    w_first,
    w_second,
    send_index,
    halo_index,
    hub_rows,
    tile_cols,
    tile_vals,
):
    routes = send_index[0]
    owned_hubs = hub_rows[0]
    rows = feats.shape[0]

    agg_grad = lax.dot_general(
        grad_out, w_second, (((1,), (1,)), ((), ())), preferred_element_type=jnp.float32
    ).astype(jnp.bfloat16)
    n_hub = lax.axis_size("group") * owned_hubs.shape[0]
    source_tiles = (V_DEV + HALO + n_hub) // TILE
    tile_terms = jnp.einsum(
        "rtij,rid->rtjd",
        tile_vals,
        agg_grad.reshape(-1, TILE, D),
        preferred_element_type=jnp.float32,
    )
    selector = (
        tile_cols[:, :, None] == jnp.arange(source_tiles, dtype=jnp.int32)[None, None, :]
    ).astype(jnp.float32)
    spread = jnp.einsum(
        "rts,rtjd->sjd", selector, tile_terms, precision=lax.Precision.HIGHEST
    ).reshape(-1, D)
    own_grad = spread[:V_DEV]
    hub_grad = lax.psum_scatter(spread[V_DEV + HALO :], "group", scatter_dimension=0, tiled=True)
    vertex_grad = own_grad.at[owned_hubs].add(hub_grad)

    both_slots = lax.all_to_all(
        jnp.stack([feats[routes], history[routes]], axis=1), "dom", split_axis=0, concat_axis=0, tiled=True
    )
    feat_slots = both_slots[:, 0]
    hist_slots = both_slots[:, 1]
    hub_first = gather_hubs(feats[owned_hubs])
    feat_halo = feat_slots.reshape(-1, D)[halo_index]
    agg_first = combine_tiles(feats, feat_halo, hub_first, tile_cols, tile_vals)
    z_first = jnp.dot(agg_first, w_first, preferred_element_type=jnp.float32)
    new_history = jax.nn.silu(z_first).astype(jnp.bfloat16)
    gate_value = jax.nn.sigmoid(z_first)
    dz_first = (vertex_grad * gate_value * (1.0 + z_first * (1.0 - gate_value))).astype(
        jnp.bfloat16
    )
    product_first = pair_product(dz_first, agg_first)
    product_first, new_history = lax.optimization_barrier((product_first, new_history))
    outgoing_first = reduce_in_group(product_first)

    hist_halo = hist_slots.reshape(-1, D)[halo_index]
    hub_second = gather_hubs(new_history[owned_hubs])
    agg_second = combine_tiles(new_history, hist_halo, hub_second, tile_cols, tile_vals)
    outgoing_second = reduce_in_group(pair_product(grad_out, agg_second))
    both = reduce_over_dom(jnp.concatenate([outgoing_first, outgoing_second], axis=1), rows)
    grad_first, grad_second = jnp.split(both, 2, axis=0)
    return (new_history, vertex_grad.astype(jnp.bfloat16), grad_first, grad_second)


def solution(mesh):
    placed = (
        P(("group", "dom"), None),
        P(("group", "dom"), None),
        P(("group", "dom"), None),
        P(),
        P(),
        P(("group", "dom"), None, None),
        P(("group", "dom")),
        P(("group", "dom"), None),
        P(("group", "dom"), None),
        P(("group", "dom"), None, None, None),
    )
    return jax.shard_map(
        on_device,
        mesh=mesh,
        in_specs=placed,
        out_specs=(
            P(("group", "dom"), None),
            P(("group", "dom"), None),
            P(("group", "dom"), None),
            P(("group", "dom"), None),
        ),
        check_vma=False,
    )
```

```python
import math

import jax
import jax.numpy as jnp
from jax import lax
from jax.sharding import PartitionSpec as P

D = 1024
V_DEV = 128
TILE = 128
HALO = 512


def combine_tiles(own_rows, halo_rows, hub_panel, tile_cols, tile_vals):
    source = jnp.concatenate([own_rows, halo_rows, hub_panel], axis=0)
    feature_width = source.shape[1]
    picked = source.reshape(-1, tile_vals.shape[2], feature_width)[tile_cols]
    summed = jnp.einsum("rtij,rtjd->rid", tile_vals, picked, preferred_element_type=jnp.float32)
    return summed.reshape(-1, feature_width).astype(jnp.bfloat16)


def weight_product(left_rows, right_rows):
    return lax.dot_general(
        left_rows, right_rows, (((0,), (0,)), ((), ())), preferred_element_type=jnp.float32
    )


def pair_product(left_rows, right_rows, flip):
    n_group = lax.axis_size("group")
    n_dom = lax.axis_size("dom")
    core = (lax.axis_index("dom") + flip) % 2
    columns = left_rows.reshape(left_rows.shape[0], n_group, n_dom // 2, 2, -1)
    keep = lax.dynamic_index_in_dim(columns, core, axis=3, keepdims=False)
    give = lax.dynamic_index_in_dim(columns, 1 - core, axis=3, keepdims=False)
    kept = weight_product(keep.reshape(left_rows.shape[0], -1), right_rows)
    sent = weight_product(give.reshape(left_rows.shape[0], -1), right_rows)
    return kept + lax.ppermute(sent, "dom", [(i, i ^ 1) for i in range(n_dom)])


def reduce_in_group(pair):
    n_group = lax.axis_size("group")
    width = pair.shape[1]
    in_group = lax.psum_scatter(pair.reshape(n_group, -1, width), "group", scatter_dimension=0, tiled=True)
    return in_group.reshape(lax.axis_size("dom") // 2, -1, width)


def reduce_over_dom(first, second, rows_per_device):
    factor = 1.0 / math.sqrt(rows_per_device * lax.axis_size("group") * lax.axis_size("dom"))
    n_dom = lax.axis_size("dom")
    width = first.shape[-1]
    core = lax.axis_index("dom") % 2
    slot = jnp.arange(2, dtype=jnp.int32)[None, :, None, None] == core
    outgoing = jnp.where(slot, first[:, None], second[:, None]).reshape(n_dom, -1, width)
    pieces = lax.all_to_all(outgoing, "dom", split_axis=0, concat_axis=0, tiled=True)
    pieces = pieces.reshape(n_dom // 2, 2, -1, width)
    own_core = lax.dynamic_index_in_dim(pieces, core, axis=1, keepdims=False)
    other_core = lax.dynamic_index_in_dim(pieces, 1 - core, axis=1, keepdims=False)
    return own_core.sum(axis=0) * factor, other_core.sum(axis=0) * factor


def gather_hubs(hub_rows):
    n_group = lax.axis_size("group")
    copies = jnp.broadcast_to(hub_rows[None], (n_group,) + hub_rows.shape)
    spread = lax.all_to_all(copies, "group", split_axis=0, concat_axis=0, tiled=True)
    return spread.reshape(-1, hub_rows.shape[1])


def on_device(
    feats,
    history,
    grad_out,
    w_first,
    w_second,
    send_index,
    halo_index,
    hub_rows,
    tile_cols,
    tile_vals,
):
    routes = send_index[0]
    owned_hubs = hub_rows[0]
    rows = feats.shape[0]

    agg_grad = lax.dot_general(
        grad_out, w_second, (((1,), (1,)), ((), ())), preferred_element_type=jnp.float32
    ).astype(jnp.bfloat16)
    n_hub = lax.axis_size("group") * owned_hubs.shape[0]
    source_tiles = (V_DEV + HALO + n_hub) // TILE
    tile_terms = jnp.einsum(
        "rtij,rid->rtjd",
        tile_vals,
        agg_grad.reshape(-1, TILE, D),
        preferred_element_type=jnp.float32,
    )
    selector = (
        tile_cols[:, :, None] == jnp.arange(source_tiles, dtype=jnp.int32)[None, None, :]
    ).astype(jnp.float32)
    spread = jnp.einsum(
        "rts,rtjd->sjd", selector, tile_terms, precision=lax.Precision.HIGHEST
    ).reshape(-1, D)
    own_grad = spread[:V_DEV]
    hub_grad = lax.psum_scatter(spread[V_DEV + HALO :], "group", scatter_dimension=0, tiled=True)
    vertex_grad = own_grad.at[owned_hubs].add(hub_grad)

    both_slots = lax.all_to_all(
        jnp.stack([feats[routes], history[routes]], axis=1), "dom", split_axis=0, concat_axis=0, tiled=True
    )
    feat_slots = both_slots[:, 0]
    hist_slots = both_slots[:, 1]
    hub_first = gather_hubs(feats[owned_hubs])
    feat_halo = feat_slots.reshape(-1, D)[halo_index]
    agg_first = combine_tiles(feats, feat_halo, hub_first, tile_cols, tile_vals)
    z_first = jnp.dot(agg_first, w_first, preferred_element_type=jnp.float32)
    new_history = jax.nn.silu(z_first).astype(jnp.bfloat16)
    gate_value = jax.nn.sigmoid(z_first)
    dz_first = (vertex_grad * gate_value * (1.0 + z_first * (1.0 - gate_value))).astype(
        jnp.bfloat16
    )
    product_first = pair_product(dz_first, agg_first, 0)
    product_first, new_history = lax.optimization_barrier((product_first, new_history))
    outgoing_first = reduce_in_group(product_first)

    hist_halo = hist_slots.reshape(-1, D)[halo_index]
    hub_second = gather_hubs(new_history[owned_hubs])
    agg_second = combine_tiles(new_history, hist_halo, hub_second, tile_cols, tile_vals)
    outgoing_second = reduce_in_group(pair_product(grad_out, agg_second, 1))
    grad_first, grad_second = reduce_over_dom(outgoing_first, outgoing_second, rows)
    return (new_history, vertex_grad.astype(jnp.bfloat16), grad_first, grad_second)


def solution(mesh):
    placed = (
        P(("group", "dom"), None),
        P(("group", "dom"), None),
        P(("group", "dom"), None),
        P(),
        P(),
        P(("group", "dom"), None, None),
        P(("group", "dom")),
        P(("group", "dom"), None),
        P(("group", "dom"), None),
        P(("group", "dom"), None, None, None),
    )
    return jax.shard_map(
        on_device,
        mesh=mesh,
        in_specs=placed,
        out_specs=(
            P(("group", "dom"), None),
            P(("group", "dom"), None),
            P(("group", "dom"), None),
            P(("group", "dom"), None),
        ),
        check_vma=False,
    )
```

```python
import math

import jax
import jax.numpy as jnp
from jax import lax
from jax.sharding import PartitionSpec as P

D = 1024
V_DEV = 128
TILE = 128
HALO = 512


def combine_tiles(own_rows, halo_rows, hub_panel, tile_cols, tile_vals):
    source = jnp.concatenate([own_rows, halo_rows, hub_panel], axis=0)
    feature_width = source.shape[1]
    picked = source.reshape(-1, tile_vals.shape[2], feature_width)[tile_cols]
    summed = jnp.einsum("rtij,rtjd->rid", tile_vals, picked, preferred_element_type=jnp.float32)
    return summed.reshape(-1, feature_width).astype(jnp.bfloat16)


def weight_product(left_rows, right_rows):
    return lax.dot_general(
        left_rows, right_rows, (((0,), (0,)), ((), ())), preferred_element_type=jnp.float32
    )


def pair_product(left_rows, right_rows, flip):
    n_group = lax.axis_size("group")
    n_dom = lax.axis_size("dom")
    core = (lax.axis_index("dom") + flip) % 2
    columns = left_rows.reshape(left_rows.shape[0], n_group, n_dom // 2, 2, -1)
    keep = lax.dynamic_index_in_dim(columns, core, axis=3, keepdims=False)
    give = lax.dynamic_index_in_dim(columns, 1 - core, axis=3, keepdims=False)
    kept = weight_product(keep.reshape(left_rows.shape[0], -1), right_rows)
    sent = weight_product(give.reshape(left_rows.shape[0], -1), right_rows)
    return kept + lax.ppermute(sent, "dom", [(i, i ^ 1) for i in range(n_dom)])


def reduce_in_group(pair):
    n_group = lax.axis_size("group")
    width = pair.shape[1]
    in_group = lax.psum_scatter(pair.reshape(n_group, -1, width), "group", scatter_dimension=0, tiled=True)
    return in_group.reshape(lax.axis_size("dom") // 2, -1, width)


def reduce_over_dom(first, second, rows_per_device):
    factor = 1.0 / math.sqrt(rows_per_device * lax.axis_size("group") * lax.axis_size("dom"))
    n_dom = lax.axis_size("dom")
    width = first.shape[-1]
    core = lax.axis_index("dom") % 2
    slot = jnp.arange(2, dtype=jnp.int32)[None, :, None, None] == core
    outgoing = jnp.where(slot, first[:, None], second[:, None]).reshape(n_dom, -1, width)
    pieces = lax.all_to_all(outgoing, "dom", split_axis=0, concat_axis=0, tiled=True)
    pieces = pieces.reshape(n_dom // 2, 2, -1, width)
    own_core = lax.dynamic_index_in_dim(pieces, core, axis=1, keepdims=False)
    other_core = lax.dynamic_index_in_dim(pieces, 1 - core, axis=1, keepdims=False)
    return own_core.sum(axis=0) * factor, other_core.sum(axis=0) * factor


def gather_hubs(hub_rows):
    n_group = lax.axis_size("group")
    copies = jnp.broadcast_to(hub_rows[None], (n_group,) + hub_rows.shape)
    spread = lax.all_to_all(copies, "group", split_axis=0, concat_axis=0, tiled=True)
    return spread.reshape(-1, hub_rows.shape[1])


def on_device(
    feats,
    history,
    grad_out,
    w_first,
    w_second,
    send_index,
    halo_index,
    hub_rows,
    tile_cols,
    tile_vals,
):
    routes = send_index[0]
    owned_hubs = hub_rows[0]
    rows = feats.shape[0]

    agg_grad = lax.dot_general(
        grad_out, w_second, (((1,), (1,)), ((), ())), preferred_element_type=jnp.float32
    ).astype(jnp.bfloat16)
    n_hub = lax.axis_size("group") * owned_hubs.shape[0]
    source_tiles = (V_DEV + HALO + n_hub) // TILE
    tile_terms = jnp.einsum(
        "rtij,rid->rtjd",
        tile_vals,
        jnp.concatenate([agg_grad, grad_out], axis=1).reshape(-1, TILE, 2 * D),
        preferred_element_type=jnp.float32,
    )
    selector = (
        tile_cols[:, :, None] == jnp.arange(source_tiles, dtype=jnp.int32)[None, None, :]
    ).astype(jnp.float32)
    spread = jnp.einsum(
        "rts,rtjd->sjd", selector, tile_terms, precision=lax.Precision.HIGHEST
    ).reshape(-1, 2 * D)
    hub_sums = lax.psum_scatter(spread[V_DEV + HALO :], "group", scatter_dimension=0, tiled=True)
    own_terms = spread[:V_DEV].at[owned_hubs].add(hub_sums)
    vertex_grad = own_terms[:, :D]
    own_weights = own_terms[:, D:]
    halo_weights = spread[V_DEV : V_DEV + HALO, D:]

    both_slots = lax.all_to_all(
        jnp.stack([feats[routes], history[routes]], axis=1), "dom", split_axis=0, concat_axis=0, tiled=True
    )
    feat_halo = both_slots[:, 0].reshape(-1, D)[halo_index]
    hist_halo = both_slots[:, 1].reshape(-1, D)[halo_index]
    hub_first = gather_hubs(feats[owned_hubs])
    agg_first = combine_tiles(feats, feat_halo, hub_first, tile_cols, tile_vals)
    z_first = jnp.dot(agg_first, w_first, preferred_element_type=jnp.float32)
    new_history = jax.nn.silu(z_first).astype(jnp.bfloat16)
    gate_value = jax.nn.sigmoid(z_first)
    dz_first = (vertex_grad * gate_value * (1.0 + z_first * (1.0 - gate_value))).astype(
        jnp.bfloat16
    )
    outgoing_first = reduce_in_group(pair_product(dz_first, agg_first, 0))

    weights = jnp.concatenate([own_weights, halo_weights], axis=0)
    weights_high = weights.astype(jnp.bfloat16)
    weights_low = (weights - weights_high.astype(jnp.float32)).astype(jnp.bfloat16)
    sources = jnp.concatenate([new_history, hist_halo], axis=0)
    outgoing_second = reduce_in_group(
        pair_product(
            jnp.concatenate([weights_high, weights_low], axis=0),
            jnp.concatenate([sources, sources], axis=0),
            1,
        )
    )
    grad_first, grad_second = reduce_over_dom(outgoing_first, outgoing_second, rows)
    return (new_history, vertex_grad.astype(jnp.bfloat16), grad_first, grad_second)


def solution(mesh):
    placed = (
        P(("group", "dom"), None),
        P(("group", "dom"), None),
        P(("group", "dom"), None),
        P(),
        P(),
        P(("group", "dom"), None, None),
        P(("group", "dom")),
        P(("group", "dom"), None),
        P(("group", "dom"), None),
        P(("group", "dom"), None, None, None),
    )
    return jax.shard_map(
        on_device,
        mesh=mesh,
        in_specs=placed,
        out_specs=(
            P(("group", "dom"), None),
            P(("group", "dom"), None),
            P(("group", "dom"), None),
            P(("group", "dom"), None),
        ),
        check_vma=False,
    )
```

```python
import math

import jax
import jax.numpy as jnp
from jax import lax
from jax.sharding import PartitionSpec as P

D = 1024
V_DEV = 128
TILE = 128
HALO = 512


def combine_tiles(own_rows, halo_rows, hub_panel, tile_cols, tile_vals):
    source = jnp.concatenate([own_rows, halo_rows, hub_panel], axis=0)
    feature_width = source.shape[1]
    picked = source.reshape(-1, tile_vals.shape[2], feature_width)[tile_cols]
    summed = jnp.einsum("rtij,rtjd->rid", tile_vals, picked, preferred_element_type=jnp.float32)
    return summed.reshape(-1, feature_width).astype(jnp.bfloat16)


def weight_product(left_rows, right_rows):
    return lax.dot_general(
        left_rows, right_rows, (((0,), (0,)), ((), ())), preferred_element_type=jnp.float32
    )


def pair_product(left_rows, right_rows, flip):
    n_group = lax.axis_size("group")
    n_dom = lax.axis_size("dom")
    core = (lax.axis_index("dom") + flip) % 2
    columns = left_rows.reshape(left_rows.shape[0], n_group, n_dom // 2, 2, -1)
    keep = lax.dynamic_index_in_dim(columns, core, axis=3, keepdims=False)
    give = lax.dynamic_index_in_dim(columns, 1 - core, axis=3, keepdims=False)
    kept = weight_product(keep.reshape(left_rows.shape[0], -1), right_rows)
    sent = weight_product(give.reshape(left_rows.shape[0], -1), right_rows)
    return kept + lax.ppermute(sent, "dom", [(i, i ^ 1) for i in range(n_dom)])


def reduce_in_group(pair, split=False):
    n_group = lax.axis_size("group")
    width = pair.shape[1]
    blocks = pair.reshape(n_group, -1, width)
    if split:
        half = width // 2
        scattered = lax.psum_scatter(blocks[:, :, :half], "group", scatter_dimension=0, tiled=True)
        exchanged = lax.all_to_all(blocks[:, :, half:], "group", split_axis=0, concat_axis=0, tiled=True)
        in_group = jnp.concatenate([scattered[0], exchanged.sum(axis=0)], axis=1)
    else:
        in_group = lax.psum_scatter(blocks, "group", scatter_dimension=0, tiled=True)
    return in_group.reshape(lax.axis_size("dom") // 2, -1, width)


def reduce_over_dom(first, second, rows_per_device):
    factor = 1.0 / math.sqrt(rows_per_device * lax.axis_size("group") * lax.axis_size("dom"))
    n_dom = lax.axis_size("dom")
    width = first.shape[-1]
    core = lax.axis_index("dom") % 2
    slot = jnp.arange(2, dtype=jnp.int32)[None, :, None, None] == core
    outgoing = jnp.where(slot, first[:, None], second[:, None]).reshape(n_dom, -1, width)
    pieces = lax.all_to_all(outgoing, "dom", split_axis=0, concat_axis=0, tiled=True)
    pieces = pieces.reshape(n_dom // 2, 2, -1, width)
    own_core = lax.dynamic_index_in_dim(pieces, core, axis=1, keepdims=False)
    other_core = lax.dynamic_index_in_dim(pieces, 1 - core, axis=1, keepdims=False)
    return own_core.sum(axis=0) * factor, other_core.sum(axis=0) * factor


def gather_hubs(hub_rows):
    n_group = lax.axis_size("group")
    copies = jnp.broadcast_to(hub_rows[None], (n_group,) + hub_rows.shape)
    spread = lax.all_to_all(copies, "group", split_axis=0, concat_axis=0, tiled=True)
    return spread.reshape(-1, hub_rows.shape[1])


def on_device(
    feats,
    history,
    grad_out,
    w_first,
    w_second,
    send_index,
    halo_index,
    hub_rows,
    tile_cols,
    tile_vals,
):
    routes = send_index[0]
    owned_hubs = hub_rows[0]
    rows = feats.shape[0]

    agg_grad = lax.dot_general(
        grad_out, w_second, (((1,), (1,)), ((), ())), preferred_element_type=jnp.float32
    ).astype(jnp.bfloat16)
    n_hub = lax.axis_size("group") * owned_hubs.shape[0]
    source_tiles = (V_DEV + HALO + n_hub) // TILE
    tile_terms = jnp.einsum(
        "rtij,rid->rtjd",
        tile_vals,
        agg_grad.reshape(-1, TILE, D),
        preferred_element_type=jnp.float32,
    )
    selector = (
        tile_cols[:, :, None] == jnp.arange(source_tiles, dtype=jnp.int32)[None, None, :]
    ).astype(jnp.float32)
    spread = jnp.einsum(
        "rts,rtjd->sjd", selector, tile_terms, precision=lax.Precision.HIGHEST
    ).reshape(-1, D)
    own_grad = spread[:V_DEV]
    hub_grad = lax.psum_scatter(spread[V_DEV + HALO :], "group", scatter_dimension=0, tiled=True)
    vertex_grad = own_grad.at[owned_hubs].add(hub_grad)

    both_slots = lax.all_to_all(
        jnp.stack([feats[routes], history[routes]], axis=1), "dom", split_axis=0, concat_axis=0, tiled=True
    )
    feat_slots = both_slots[:, 0]
    hist_slots = both_slots[:, 1]
    hub_first = gather_hubs(feats[owned_hubs])
    feat_halo = feat_slots.reshape(-1, D)[halo_index]
    agg_first = combine_tiles(feats, feat_halo, hub_first, tile_cols, tile_vals)
    z_first = jnp.dot(agg_first, w_first, preferred_element_type=jnp.float32)
    new_history = jax.nn.silu(z_first).astype(jnp.bfloat16)
    gate_value = jax.nn.sigmoid(z_first)
    dz_first = (vertex_grad * gate_value * (1.0 + z_first * (1.0 - gate_value))).astype(
        jnp.bfloat16
    )
    product_first = pair_product(dz_first, agg_first, 0)
    product_first, new_history = lax.optimization_barrier((product_first, new_history))
    outgoing_first = reduce_in_group(product_first)

    hist_halo = hist_slots.reshape(-1, D)[halo_index]
    hub_second = gather_hubs(new_history[owned_hubs])
    agg_second = combine_tiles(new_history, hist_halo, hub_second, tile_cols, tile_vals)
    outgoing_second = reduce_in_group(pair_product(grad_out, agg_second, 1), split=True)
    grad_first, grad_second = reduce_over_dom(outgoing_first, outgoing_second, rows)
    return (new_history, vertex_grad.astype(jnp.bfloat16), grad_first, grad_second)


def solution(mesh):
    placed = (
        P(("group", "dom"), None),
        P(("group", "dom"), None),
        P(("group", "dom"), None),
        P(),
        P(),
        P(("group", "dom"), None, None),
        P(("group", "dom")),
        P(("group", "dom"), None),
        P(("group", "dom"), None),
        P(("group", "dom"), None, None, None),
    )
    return jax.shard_map(
        on_device,
        mesh=mesh,
        in_specs=placed,
        out_specs=(
            P(("group", "dom"), None),
            P(("group", "dom"), None),
            P(("group", "dom"), None),
            P(("group", "dom"), None),
        ),
        check_vma=False,
    )
```

```python
import math

import jax
import jax.numpy as jnp
from jax import lax
from jax.sharding import PartitionSpec as P

D = 1024
V_DEV = 128
TILE = 128
HALO = 512


def combine_tiles(own_rows, halo_rows, hub_panel, tile_cols, tile_vals):
    source = jnp.concatenate([own_rows, halo_rows, hub_panel], axis=0)
    feature_width = source.shape[1]
    picked = source.reshape(-1, tile_vals.shape[2], feature_width)[tile_cols]
    summed = jnp.einsum("rtij,rtjd->rid", tile_vals, picked, preferred_element_type=jnp.float32)
    return summed.reshape(-1, feature_width).astype(jnp.bfloat16)


def weight_product(left_rows, right_rows):
    return lax.dot_general(
        left_rows, right_rows, (((0,), (0,)), ((), ())), preferred_element_type=jnp.float32
    )


def pair_product(left_rows, right_rows, flip):
    n_group = lax.axis_size("group")
    n_dom = lax.axis_size("dom")
    core = (lax.axis_index("dom") + flip) % 2
    columns = left_rows.reshape(left_rows.shape[0], n_group, n_dom // 2, 2, -1)
    keep = lax.dynamic_index_in_dim(columns, core, axis=3, keepdims=False)
    give = lax.dynamic_index_in_dim(columns, 1 - core, axis=3, keepdims=False)
    kept = weight_product(keep.reshape(left_rows.shape[0], -1), right_rows)
    sent = weight_product(give.reshape(left_rows.shape[0], -1), right_rows)
    return kept + lax.ppermute(sent, "dom", [(i, i ^ 1) for i in range(n_dom)])


def reduce_in_group(pair):
    n_group = lax.axis_size("group")
    width = pair.shape[1]
    in_group = lax.psum_scatter(pair.reshape(n_group, -1, width), "group", scatter_dimension=0, tiled=True)
    return in_group.reshape(lax.axis_size("dom") // 2, -1, width)


def reduce_over_dom(first, second, rows_per_device):
    factor = 1.0 / math.sqrt(rows_per_device * lax.axis_size("group") * lax.axis_size("dom"))
    n_dom = lax.axis_size("dom")
    width = first.shape[-1]
    core = lax.axis_index("dom") % 2
    slot = jnp.arange(2, dtype=jnp.int32)[None, :, None, None] == core
    outgoing = jnp.where(slot, first[:, None], second[:, None]).reshape(n_dom, -1, width)
    pieces = lax.all_to_all(outgoing, "dom", split_axis=0, concat_axis=0, tiled=True)
    pieces = pieces.reshape(n_dom // 2, 2, -1, width)
    own_core = lax.dynamic_index_in_dim(pieces, core, axis=1, keepdims=False)
    other_core = lax.dynamic_index_in_dim(pieces, 1 - core, axis=1, keepdims=False)
    return own_core.sum(axis=0) * factor, other_core.sum(axis=0) * factor


def gather_hubs(hub_rows):
    n_group = lax.axis_size("group")
    shifted = [hub_rows] + [
        lax.ppermute(hub_rows, "group", [(i, (i + s) % n_group) for i in range(n_group)])
        for s in range(1, n_group)
    ]
    by_shift = jnp.stack(shifted, axis=0)
    shift_of_source = (lax.axis_index("group") - jnp.arange(n_group, dtype=jnp.int32)) % n_group
    return jnp.take(by_shift, shift_of_source, axis=0).reshape(-1, hub_rows.shape[1])


def on_device(
    feats,
    history,
    grad_out,
    w_first,
    w_second,
    send_index,
    halo_index,
    hub_rows,
    tile_cols,
    tile_vals,
):
    routes = send_index[0]
    owned_hubs = hub_rows[0]
    rows = feats.shape[0]

    agg_grad = lax.dot_general(
        grad_out, w_second, (((1,), (1,)), ((), ())), preferred_element_type=jnp.float32
    ).astype(jnp.bfloat16)
    n_hub = lax.axis_size("group") * owned_hubs.shape[0]
    source_tiles = (V_DEV + HALO + n_hub) // TILE
    tile_terms = jnp.einsum(
        "rtij,rid->rtjd",
        tile_vals,
        agg_grad.reshape(-1, TILE, D),
        preferred_element_type=jnp.float32,
    )
    selector = (
        tile_cols[:, :, None] == jnp.arange(source_tiles, dtype=jnp.int32)[None, None, :]
    ).astype(jnp.float32)
    spread = jnp.einsum(
        "rts,rtjd->sjd", selector, tile_terms, precision=lax.Precision.HIGHEST
    ).reshape(-1, D)
    own_grad = spread[:V_DEV]
    hub_grad = lax.psum_scatter(spread[V_DEV + HALO :], "group", scatter_dimension=0, tiled=True)
    vertex_grad = own_grad.at[owned_hubs].add(hub_grad)

    both_slots = lax.all_to_all(
        jnp.stack([feats[routes], history[routes]], axis=1), "dom", split_axis=0, concat_axis=0, tiled=True
    )
    feat_slots = both_slots[:, 0]
    hist_slots = both_slots[:, 1]
    hub_first = gather_hubs(feats[owned_hubs])
    feat_halo = feat_slots.reshape(-1, D)[halo_index]
    agg_first = combine_tiles(feats, feat_halo, hub_first, tile_cols, tile_vals)
    z_first = jnp.dot(agg_first, w_first, preferred_element_type=jnp.float32)
    new_history = jax.nn.silu(z_first).astype(jnp.bfloat16)
    gate_value = jax.nn.sigmoid(z_first)
    dz_first = (vertex_grad * gate_value * (1.0 + z_first * (1.0 - gate_value))).astype(
        jnp.bfloat16
    )
    product_first = pair_product(dz_first, agg_first, 0)
    product_first, new_history = lax.optimization_barrier((product_first, new_history))
    outgoing_first = reduce_in_group(product_first)

    hist_halo = hist_slots.reshape(-1, D)[halo_index]
    hub_second = gather_hubs(new_history[owned_hubs])
    agg_second = combine_tiles(new_history, hist_halo, hub_second, tile_cols, tile_vals)
    outgoing_second = reduce_in_group(pair_product(grad_out, agg_second, 1))
    grad_first, grad_second = reduce_over_dom(outgoing_first, outgoing_second, rows)
    return (new_history, vertex_grad.astype(jnp.bfloat16), grad_first, grad_second)


def solution(mesh):
    placed = (
        P(("group", "dom"), None),
        P(("group", "dom"), None),
        P(("group", "dom"), None),
        P(),
        P(),
        P(("group", "dom"), None, None),
        P(("group", "dom")),
        P(("group", "dom"), None),
        P(("group", "dom"), None),
        P(("group", "dom"), None, None, None),
    )
    return jax.shard_map(
        on_device,
        mesh=mesh,
        in_specs=placed,
        out_specs=(
            P(("group", "dom"), None),
            P(("group", "dom"), None),
            P(("group", "dom"), None),
            P(("group", "dom"), None),
        ),
        check_vma=False,
    )
```

```python
import math

import jax
import jax.numpy as jnp
from jax import lax
from jax.sharding import PartitionSpec as P

D = 1024
V_DEV = 128
TILE = 128
HALO = 512


def combine_tiles(own_rows, halo_rows, hub_panel, tile_cols, tile_vals):
    source = jnp.concatenate([own_rows, halo_rows, hub_panel], axis=0)
    feature_width = source.shape[1]
    picked = source.reshape(-1, tile_vals.shape[2], feature_width)[tile_cols]
    summed = jnp.einsum("rtij,rtjd->rid", tile_vals, picked, preferred_element_type=jnp.float32)
    return summed.reshape(-1, feature_width).astype(jnp.bfloat16)


def weight_product(left_rows, right_rows):
    return lax.dot_general(
        left_rows, right_rows, (((0,), (0,)), ((), ())), preferred_element_type=jnp.float32
    )


def pair_product(left_rows, right_rows, flip):
    n_group = lax.axis_size("group")
    n_dom = lax.axis_size("dom")
    core = (lax.axis_index("dom") + flip) % 2
    columns = left_rows.reshape(left_rows.shape[0], n_group, n_dom // 2, 2, -1)
    keep = lax.dynamic_index_in_dim(columns, core, axis=3, keepdims=False)
    give = lax.dynamic_index_in_dim(columns, 1 - core, axis=3, keepdims=False)
    kept = weight_product(keep.reshape(left_rows.shape[0], -1), right_rows)
    sent = weight_product(give.reshape(left_rows.shape[0], -1), right_rows)
    return kept + lax.ppermute(sent, "dom", [(i, i ^ 1) for i in range(n_dom)])


def reduce_in_group(pair):
    n_group = lax.axis_size("group")
    width = pair.shape[1]
    in_group = lax.psum_scatter(pair.reshape(n_group, -1, width), "group", scatter_dimension=0, tiled=True)
    return in_group.reshape(lax.axis_size("dom") // 2, -1, width)


def reduce_over_dom(first, second, rows_per_device):
    factor = 1.0 / math.sqrt(rows_per_device * lax.axis_size("group") * lax.axis_size("dom"))
    n_dom = lax.axis_size("dom")
    width = first.shape[-1]
    core = lax.axis_index("dom") % 2
    slot = jnp.arange(2, dtype=jnp.int32)[None, :, None, None] == core
    outgoing = jnp.where(slot, first[:, None], second[:, None]).reshape(n_dom, -1, width)
    pieces = lax.all_to_all(outgoing, "dom", split_axis=0, concat_axis=0, tiled=True)
    pieces = pieces.reshape(n_dom // 2, 2, -1, width)
    own_core = lax.dynamic_index_in_dim(pieces, core, axis=1, keepdims=False)
    other_core = lax.dynamic_index_in_dim(pieces, 1 - core, axis=1, keepdims=False)
    return own_core.sum(axis=0) * factor, other_core.sum(axis=0) * factor


def gather_hubs(hub_rows):
    n_group = lax.axis_size("group")
    copies = jnp.broadcast_to(hub_rows[None], (n_group,) + hub_rows.shape)
    spread = lax.all_to_all(copies, "group", split_axis=0, concat_axis=0, tiled=True)
    return spread.reshape(-1, hub_rows.shape[1])


def on_device(
    feats,
    history,
    grad_out,
    w_first,
    w_second,
    send_index,
    halo_index,
    hub_rows,
    tile_cols,
    tile_vals,
):
    routes = send_index[0]
    owned_hubs = hub_rows[0]
    rows = feats.shape[0]

    agg_grad = lax.dot_general(
        grad_out, w_second, (((1,), (1,)), ((), ())), preferred_element_type=jnp.float32
    ).astype(jnp.bfloat16)
    n_hub = lax.axis_size("group") * owned_hubs.shape[0]
    source_tiles = (V_DEV + HALO + n_hub) // TILE
    tile_terms = jnp.einsum(
        "rtij,rid->rtjd",
        tile_vals,
        agg_grad.reshape(-1, TILE, D),
        preferred_element_type=jnp.float32,
    )
    selector = (
        tile_cols[:, :, None] == jnp.arange(source_tiles, dtype=jnp.int32)[None, None, :]
    ).astype(jnp.float32)
    spread = jnp.einsum(
        "rts,rtjd->sjd", selector, tile_terms, precision=lax.Precision.HIGHEST
    ).reshape(-1, D)
    own_grad = spread[:V_DEV]
    hub_grad = lax.psum_scatter(spread[V_DEV + HALO :], "group", scatter_dimension=0, tiled=True)
    vertex_grad = own_grad.at[owned_hubs].add(hub_grad)

    both_slots = lax.all_to_all(
        jnp.stack([feats[routes], history[routes]], axis=1), "dom", split_axis=0, concat_axis=0, tiled=True
    )
    feat_slots = both_slots[:, 0]
    hist_slots = both_slots[:, 1]
    hub_first = gather_hubs(feats[owned_hubs])
    feat_halo = feat_slots.reshape(-1, D)[halo_index]
    agg_first = combine_tiles(feats, feat_halo, hub_first, tile_cols, tile_vals)
    z_first = jnp.dot(agg_first, w_first, preferred_element_type=jnp.float32)
    new_history = jax.nn.silu(z_first).astype(jnp.bfloat16)
    gate_value = jax.nn.sigmoid(z_first)
    dz_first = (vertex_grad * gate_value * (1.0 + z_first * (1.0 - gate_value))).astype(
        jnp.bfloat16
    )
    product_first = pair_product(dz_first, agg_first, 0)

    hist_halo = hist_slots.reshape(-1, D)[halo_index]
    hub_second = gather_hubs(new_history[owned_hubs])
    agg_second = combine_tiles(new_history, hist_halo, hub_second, tile_cols, tile_vals)
    product_second = pair_product(grad_out, agg_second, 1)
    n_group = lax.axis_size("group")
    both = jnp.concatenate(
        [product_first.reshape(n_group, -1, D), product_second.reshape(n_group, -1, D)], axis=1
    )
    outgoing = reduce_in_group(both.reshape(-1, D)).reshape(2, lax.axis_size("dom") // 2, -1, D)
    grad_first, grad_second = reduce_over_dom(outgoing[0], outgoing[1], rows)
    return (new_history, vertex_grad.astype(jnp.bfloat16), grad_first, grad_second)


def solution(mesh):
    placed = (
        P(("group", "dom"), None),
        P(("group", "dom"), None),
        P(("group", "dom"), None),
        P(),
        P(),
        P(("group", "dom"), None, None),
        P(("group", "dom")),
        P(("group", "dom"), None),
        P(("group", "dom"), None),
        P(("group", "dom"), None, None, None),
    )
    return jax.shard_map(
        on_device,
        mesh=mesh,
        in_specs=placed,
        out_specs=(
            P(("group", "dom"), None),
            P(("group", "dom"), None),
            P(("group", "dom"), None),
            P(("group", "dom"), None),
        ),
        check_vma=False,
    )
```

```python
import math

import jax
import jax.numpy as jnp
from jax import lax
from jax.sharding import PartitionSpec as P

D = 1024
V_DEV = 128
TILE = 128
HALO = 512


def combine_tiles(own_rows, halo_rows, hub_panel, tile_cols, tile_vals):
    source = jnp.concatenate([own_rows, halo_rows, hub_panel], axis=0)
    feature_width = source.shape[1]
    picked = source.reshape(-1, tile_vals.shape[2], feature_width)[tile_cols]
    summed = jnp.einsum("rtij,rtjd->rid", tile_vals, picked, preferred_element_type=jnp.float32)
    return summed.reshape(-1, feature_width).astype(jnp.bfloat16)


def weight_product(left_rows, right_rows):
    return lax.dot_general(
        left_rows, right_rows, (((0,), (0,)), ((), ())), preferred_element_type=jnp.float32
    )


def pair_product(left_rows, right_rows, flip):
    n_group = lax.axis_size("group")
    n_dom = lax.axis_size("dom")
    core = (lax.axis_index("dom") + flip) % 2
    columns = left_rows.reshape(left_rows.shape[0], n_group, n_dom // 2, 2, -1)
    keep = lax.dynamic_index_in_dim(columns, core, axis=3, keepdims=False)
    give = lax.dynamic_index_in_dim(columns, 1 - core, axis=3, keepdims=False)
    kept = weight_product(keep.reshape(left_rows.shape[0], -1), right_rows)
    sent = weight_product(give.reshape(left_rows.shape[0], -1), right_rows)
    return kept + lax.ppermute(sent, "dom", [(i, i ^ 1) for i in range(n_dom)])


def reduce_in_group(pair):
    n_group = lax.axis_size("group")
    width = pair.shape[1]
    in_group = lax.psum_scatter(pair.reshape(n_group, -1, width), "group", scatter_dimension=0, tiled=True)
    return in_group.reshape(lax.axis_size("dom") // 2, -1, width)


def reduce_over_dom(first, second, rows_per_device):
    factor = 1.0 / math.sqrt(rows_per_device * lax.axis_size("group") * lax.axis_size("dom"))
    n_dom = lax.axis_size("dom")
    width = first.shape[-1]
    core = lax.axis_index("dom") % 2
    slot = jnp.arange(2, dtype=jnp.int32)[None, :, None, None] == core
    outgoing = jnp.where(slot, first[:, None], second[:, None]).reshape(n_dom, -1, width)
    pieces = lax.all_to_all(outgoing, "dom", split_axis=0, concat_axis=0, tiled=True)
    pieces = pieces.reshape(n_dom // 2, 2, -1, width)
    own_core = lax.dynamic_index_in_dim(pieces, core, axis=1, keepdims=False)
    other_core = lax.dynamic_index_in_dim(pieces, 1 - core, axis=1, keepdims=False)
    return own_core.sum(axis=0) * factor, other_core.sum(axis=0) * factor


def gather_hubs(hub_rows):
    n_group = lax.axis_size("group")
    copies = jnp.broadcast_to(hub_rows[None], (n_group,) + hub_rows.shape)
    spread = lax.all_to_all(copies, "group", split_axis=0, concat_axis=0, tiled=True)
    return spread.reshape(-1, hub_rows.shape[1])


def on_device(
    feats,
    history,
    grad_out,
    w_first,
    w_second,
    send_index,
    halo_index,
    hub_rows,
    tile_cols,
    tile_vals,
):
    routes = send_index[0]
    owned_hubs = hub_rows[0]
    rows = feats.shape[0]

    agg_grad = lax.dot_general(
        grad_out, w_second, (((1,), (1,)), ((), ())), preferred_element_type=jnp.float32
    ).astype(jnp.bfloat16)
    n_hub = lax.axis_size("group") * owned_hubs.shape[0]
    source_tiles = (V_DEV + HALO + n_hub) // TILE
    tile_terms = jnp.einsum(
        "rtij,rid->rtjd",
        tile_vals,
        agg_grad.reshape(-1, TILE, D),
        preferred_element_type=jnp.float32,
    )
    selector = (
        tile_cols[:, :, None] == jnp.arange(source_tiles, dtype=jnp.int32)[None, None, :]
    ).astype(jnp.float32)
    spread = jnp.einsum(
        "rts,rtjd->sjd", selector, tile_terms, precision=lax.Precision.HIGHEST
    ).reshape(-1, D)
    own_grad = spread[:V_DEV]
    hub_grad = lax.psum_scatter(spread[V_DEV + HALO :], "group", scatter_dimension=0, tiled=True)
    vertex_grad = own_grad.at[owned_hubs].add(hub_grad)

    feat_slots = lax.all_to_all(feats[routes], "dom", split_axis=0, concat_axis=0, tiled=True)
    hist_slots = lax.all_to_all(history[routes], "dom", split_axis=0, concat_axis=0, tiled=True)
    hub_first = gather_hubs(feats[owned_hubs])
    feat_halo = feat_slots.reshape(-1, D)[halo_index]
    agg_first = combine_tiles(feats, feat_halo, hub_first, tile_cols, tile_vals)
    z_first = jnp.dot(agg_first, w_first, preferred_element_type=jnp.float32)
    new_history = jax.nn.silu(z_first).astype(jnp.bfloat16)
    gate_value = jax.nn.sigmoid(z_first)
    dz_first = (vertex_grad * gate_value * (1.0 + z_first * (1.0 - gate_value))).astype(
        jnp.bfloat16
    )
    product_first = pair_product(dz_first, agg_first, 0)

    hist_halo = hist_slots.reshape(-1, D)[halo_index]
    hub_second = gather_hubs(new_history[owned_hubs])
    agg_second = combine_tiles(new_history, hist_halo, hub_second, tile_cols, tile_vals)
    product_second = pair_product(grad_out, agg_second, 1)
    n_group = lax.axis_size("group")
    both = jnp.concatenate(
        [product_first.reshape(n_group, -1, D), product_second.reshape(n_group, -1, D)], axis=1
    )
    outgoing = reduce_in_group(both.reshape(-1, D)).reshape(2, lax.axis_size("dom") // 2, -1, D)
    grad_first, grad_second = reduce_over_dom(outgoing[0], outgoing[1], rows)
    return (new_history, vertex_grad.astype(jnp.bfloat16), grad_first, grad_second)


def solution(mesh):
    placed = (
        P(("group", "dom"), None),
        P(("group", "dom"), None),
        P(("group", "dom"), None),
        P(),
        P(),
        P(("group", "dom"), None, None),
        P(("group", "dom")),
        P(("group", "dom"), None),
        P(("group", "dom"), None),
        P(("group", "dom"), None, None, None),
    )
    return jax.shard_map(
        on_device,
        mesh=mesh,
        in_specs=placed,
        out_specs=(
            P(("group", "dom"), None),
            P(("group", "dom"), None),
            P(("group", "dom"), None),
            P(("group", "dom"), None),
        ),
        check_vma=False,
    )
```
